256 devices in a mesh: ctx: 64 (over y_hi, x, z), tp: 4 (over y_lo, core).
Axes of the slice: x: 4, y: 4 (y_hi: 2, y_lo: 2; y = y_hi * 2 + y_lo), z: 8, core: 2. Of those that a mesh axis runs over, the one named last changes fastest.
Arguments:
- queries: bfloat16 [16384, 4096], P('ctx', 'tp'), may hold values from -8 to 8
- keys_values: bfloat16 [16384, 2, 512], P('ctx', None, 'tp'), may hold values from -8 to 8
- placement: int32 [2], replicated, may hold values from 1 to 63
- lengths: int32 [8], replicated, may hold values from 1 to 10922, 16384 in all
- steer_index: int32 [8], replicated, may hold values from 0 to 15
- steering: bfloat16 [16, 4096], P(None, 'tp'), may hold values from -3 to 3
Outputs:
- steered: bfloat16 [16384, 4096], P('ctx', 'tp')
The draws below stay inside these ranges and needn't reach their ends.
Inputs may be any that keep to these rules, and one draw needn't show every extreme that they name: The lengths sum to 16384 and the longest is exactly 10922.
All inputs are finite; a program needn't handle non-finite values.
Results may differ from the reference program's by a relative error of at most 0.0034.
Values may be sent and summed in bfloat16 or wider, within the bound.
No kernel may reach another device: no remote copies, remote signals or barrier semaphores. Data moves between devices by JAX's collectives and lax.ppermute only.
A program may use at most 64 MiB of HBM per device.

```python
import math
import jax
import jax.numpy as jnp
import numpy as np
from jax import lax

HEADS = 32
KVH = 4
HD = 128
NREQ = 8
NSTEER = 16
TOKENS = 16384
MOST = 10922
BQ = 512
N_CTX = 64


def draw_keys_values(key, part):
    shape_all = (TOKENS, 2, KVH * HD)
    baseline = jnp.clip(jax.random.normal(jax.random.fold_in(key, 11), shape_all, jnp.float32), -6.0, 6.0)
    return baseline.astype(jnp.bfloat16)


def draw_queries(key, part):
    shape_all = (TOKENS, HEADS * HD)
    baseline = jnp.clip(jax.random.normal(jax.random.fold_in(key, 13), shape_all, jnp.float32), -6.0, 6.0)
    return baseline.astype(jnp.bfloat16)


def plant(result, rng, low, high):
    shape = result.shape
    index_at = [jax.random.randint(jax.random.fold_in(rng, axis), (), 0, shape[axis]) for axis in range(len(shape))]
    result = result.at[tuple(index_at)].set(low)
    longest = shape.index(max(shape))
    index_at[longest] = (index_at[longest] + 1) % shape[longest]
    return result.at[tuple(index_at)].set(high)


def block_scale(rng, dims, pieces, low, top_value):
    gain = 1.0
    for dim, blocks in pieces:
        draws = jax.random.uniform(jax.random.fold_in(jax.random.fold_in(rng, 6), dim), (blocks,), jnp.float32, low / len(pieces), top_value / len(pieces))
        gain = gain * jnp.repeat(jnp.exp(draws), dims[dim] // blocks).reshape((-1,) + (1,) * (len(dims) - 1 - dim))
    return gain


def profile(count, total, limit, skew):
    portions = [(1 << 20) // math.isqrt(grade ** skew) + 1 for grade in range(2, count + 1)]
    spare, holding = total - limit - (count - 1), [1] * (count - 1)
    while spare > 0:
        movable = [i for i in range(count - 1) if holding[i] < limit]
        whole, remaining = sum([portions[i] for i in movable]), spare
        for i in movable:
            extra = min(limit - holding[i], max(1, remaining * portions[i] // whole), spare)
            holding[i] = holding[i] + extra
            spare = spare - extra
    return np.array([limit] + holding)


def ragged(own_key, amount, total, most, slope):
    if amount == 2:
        one = jax.random.randint(own_key, (), max(1, total - most), min(most, total - 1) + 1)
        return jnp.stack([one, total - one])
    sizes = jnp.asarray(profile(amount, total, most, slope), jnp.int32)
    pairs = (amount - 1) // 2
    source_of, taker = sizes[1:1 + 2 * pairs:2], sizes[2:2 + 2 * pairs:2]
    room = jnp.minimum(source_of - 1, most - taker)
    passed = jax.random.randint(jax.random.fold_in(own_key, 1), (pairs,), 0, 1 << 20) % (room + 1)
    sizes = sizes.at[1:1 + 2 * pairs:2].set(source_of - passed).at[2:2 + 2 * pairs:2].set(taker + passed)
    return sizes[jax.random.permutation(jax.random.fold_in(own_key, 2), amount)]


def gaussian(own_key, extent, scale, reach, split=(), kind=jnp.bfloat16):
    drawn = scale * jax.random.normal(own_key, extent, jnp.float32)
    if split:
        drawn = drawn * block_scale(own_key, extent, split, -0.22, 0.18)
    return jnp.clip(drawn, -reach, reach).astype(kind)


def setup_inputs(seed: int = 0) -> dict:
    arg_keys = jax.random.split(jax.random.key(seed), 7)
    queries = draw_queries(jax.random.fold_in(arg_keys[6], 71), 0)
    keys_values = draw_keys_values(jax.random.fold_in(arg_keys[6], 71), 0)
    placement = jax.random.randint(arg_keys[2], (2,), 1, N_CTX).astype(jnp.int32)
    lengths = ragged(arg_keys[3], NREQ, TOKENS, MOST, 2).astype(jnp.int32)
    steer_index = plant(jax.random.randint(arg_keys[4], (NREQ,), 0, NSTEER), jax.random.fold_in(arg_keys[4], 1), 0, NSTEER - 1).astype(jnp.int32)
    steering = gaussian(arg_keys[5], (NSTEER, HEADS * HD), 0.5, 3.0, ((1, 4),))
    return {"queries": queries, "keys_values": keys_values, "placement": placement, "lengths": lengths, "steer_index": steer_index, "steering": steering}


def packed_positions(placement, tok_rows, shards):
    shard_ids = jnp.arange(shards, dtype=jnp.int32)
    local_rows = jnp.arange(tok_rows, dtype=jnp.int32)
    half_rows = tok_rows // 2
    mask_rows = jnp.where(local_rows < half_rows, placement[0], placement[1]).astype(jnp.int32)
    owners = jnp.bitwise_xor(shard_ids[:, None], mask_rows[None, :]).astype(jnp.int32)
    return (owners * tok_rows + local_rows[None, :]).reshape(-1).astype(jnp.int32)


def request_of(positions, lengths):
    request_ends = jnp.cumsum(lengths).astype(jnp.int32)
    return jnp.sum((positions[:, None] >= request_ends[None, :]).astype(jnp.int32), axis=1).astype(jnp.int32)


def reference(queries, keys_values, placement, lengths, steer_index, steering):
    tok_rows = TOKENS // N_CTX
    positions = packed_positions(placement, tok_rows, N_CTX)
    q_packed = jnp.zeros_like(queries).at[positions].set(queries)
    kv_packed = jnp.zeros_like(keys_values).at[positions].set(keys_values)
    request = request_of(jnp.arange(TOKENS, dtype=jnp.int32), lengths)
    group_size = HEADS // KVH
    window = MOST + BQ
    scale = HD ** -0.5

    def one_block(block_index):
        row_first = (block_index * BQ).astype(jnp.int32)
        key_first = jnp.clip(row_first - MOST, 0, TOKENS - window).astype(jnp.int32)
        query_block = lax.dynamic_slice_in_dim(q_packed, row_first, BQ, 0).astype(jnp.float32).reshape(BQ, KVH, group_size, HD)
        kv_block = lax.dynamic_slice_in_dim(kv_packed, key_first, window, 0).astype(jnp.float32)
        key_rows = kv_block[:, 0].reshape(window, KVH, HD)
        value_rows = kv_block[:, 1].reshape(window, KVH, HD)
        query_pos = row_first + jnp.arange(BQ, dtype=jnp.int32)
        key_pos = key_first + jnp.arange(window, dtype=jnp.int32)
        query_request = lax.dynamic_slice_in_dim(request, row_first, BQ, 0)
        key_request = lax.dynamic_slice_in_dim(request, key_first, window, 0)
        allowed = (query_request[:, None] == key_request[None, :]) & (key_pos[None, :] <= query_pos[:, None])
        allowed = allowed[:, None, None, :]
        scores = jnp.einsum("qhgd,khd->qhgk", query_block, key_rows) * scale
        masked = jnp.where(allowed, scores, jnp.float32(-1.0e30))
        row_max = jnp.max(masked, axis=-1, keepdims=True)
        weights = jnp.where(allowed, jnp.exp(masked - row_max), jnp.float32(0.0))
        weight_total = jnp.sum(weights, axis=-1)
        rounded = lax.optimization_barrier(weights.astype(jnp.bfloat16)).astype(jnp.float32)
        mixed = jnp.einsum("qhgk,khd->qhgd", rounded, value_rows)
        return (mixed / weight_total[..., None]).reshape(BQ, HEADS * HD).astype(jnp.bfloat16)

    attended = lax.map(one_block, jnp.arange(TOKENS // BQ, dtype=jnp.int32)).reshape(TOKENS, HEADS * HD)
    chosen = jnp.sum(jnp.where(request[:, None] == jnp.arange(NREQ, dtype=jnp.int32)[None, :], steer_index[None, :], 0), axis=1).astype(jnp.int32)
    steer_rows = steering[chosen].astype(jnp.float32)
    return (attended.astype(jnp.float32) + steer_rows).astype(jnp.bfloat16)
```

```python
import functools

import jax
import jax.numpy as jnp
from jax import lax
from jax.experimental import pallas as pl
from jax.experimental.pallas import tpu as pltpu
from jax.sharding import PartitionSpec as P

HD = 128
MOST = 10922
BK = 512
negative_fill = -1e30


def partner(value, axis, bit):
    mask = 2**bit
    pairs = [(source, source ^ mask) for source in range(lax.axis_size(axis))]
    return lax.ppermute(value, axis, pairs)


def request_of(positions, lengths):
    request_ends = jnp.cumsum(lengths)
    return jnp.sum((positions[:, None] >= request_ends[None, :]).astype(jnp.int32), axis=1)


def request_start(positions, ends):
    return jnp.max(jnp.where(ends[None, :] <= positions[:, None], ends[None, :], 0), axis=1)


def attention_kernel(group, steps, info_ref, q_ref, k_ref, v_ref, steer_ref, o_ref, m_sc, l_sc, acc_sc):
    j = pl.program_id(0)
    i = pl.program_id(1)
    rows = q_ref.shape[0]
    qbase = info_ref[j * 4 + 0]
    kstart = info_ref[j * 4 + 1]
    kend = info_ref[j * 4 + 2]
    qs_max = info_ref[j * 4 + 3]
    ends = [info_ref[8 + r] for r in range(8)]
    kb = kstart + i

    @pl.when(i == 0)
    def _():
        m_sc[...] = jnp.full(m_sc.shape, negative_fill, jnp.float32)
        l_sc[...] = jnp.zeros(l_sc.shape, jnp.float32)
        acc_sc[...] = jnp.zeros(acc_sc.shape, jnp.float32)

    def step(masked):
        q = q_ref[...]
        k = k_ref[...]
        s = lax.dot_general(q, k, (((1,), (1,)), ((), ())), preferred_element_type=jnp.float32)
        s = s * (HD ** -0.5)
        if masked:
            qpos = qbase + lax.broadcasted_iota(jnp.int32, (rows, 1), 0) // group
            qstart = jnp.zeros((rows, 1), jnp.int32)
            for e in ends:
                qstart = jnp.where(e <= qpos, jnp.maximum(qstart, e), qstart)
            kpos = kb * BK + lax.broadcasted_iota(jnp.int32, (1, BK), 1)
            allowed = (kpos <= qpos) & (kpos >= qstart)
            s = jnp.where(allowed, s, negative_fill)
        m_old = m_sc[...]
        m_new = jnp.maximum(m_old, jnp.max(s, axis=1, keepdims=True))
        p = jnp.exp(s - m_new)
        if masked:
            p = jnp.where(allowed, p, 0.0)
        alpha = jnp.exp(m_old - m_new)
        l_sc[...] = alpha * l_sc[...] + jnp.sum(p, axis=1, keepdims=True)
        acc_sc[...] = alpha * acc_sc[...] + jnp.dot(
            p.astype(jnp.bfloat16), v_ref[...], preferred_element_type=jnp.float32
        )
        m_sc[...] = m_new

    live = kb <= kend
    full = (kb * BK >= qs_max) & ((kb + 1) * BK - 1 <= qbase)

    @pl.when(live & full)
    def _():
        step(False)

    @pl.when(live & jnp.logical_not(full))
    def _():
        step(True)

    @pl.when(i == steps - 1)
    def _():
        attended = (acc_sc[...] / l_sc[...]).astype(jnp.bfloat16).astype(jnp.float32)
        o_ref[...] = (attended + steer_ref[...].astype(jnp.float32)).astype(o_ref.dtype)


def attention(info, q2, k, v, steer2, group):
    rows_all = q2.shape[0]
    half = rows_all // 2
    total_blocks = k.shape[0] // BK
    steps = min(total_blocks, (MOST + half // group - 1) // BK + 2)

    def kv_map(j, i, info_ref):
        return (jnp.minimum(info_ref[j * 4 + 1] + i, info_ref[j * 4 + 2]), 0)

    grid_spec = pltpu.PrefetchScalarGridSpec(
        num_scalar_prefetch=1,
        grid=(2, steps),
        in_specs=[
            pl.BlockSpec((half, HD), lambda j, i, info_ref: (j, 0)),
            pl.BlockSpec((BK, HD), kv_map),
            pl.BlockSpec((BK, HD), kv_map),
            pl.BlockSpec((half, HD), lambda j, i, info_ref: (j, 0)),
        ],
        out_specs=pl.BlockSpec((half, HD), lambda j, i, info_ref: (j, 0)),
        scratch_shapes=[
            pltpu.VMEM((half, 1), jnp.float32),
            pltpu.VMEM((half, 1), jnp.float32),
            pltpu.VMEM((half, HD), jnp.float32),
        ],
    )
    return pl.pallas_call(
        functools.partial(attention_kernel, group, steps),
        grid_spec=grid_spec,
        out_shape=jax.ShapeDtypeStruct((rows_all, HD), jnp.bfloat16),
        compiler_params=pltpu.CompilerParams(
            dimension_semantics=("arbitrary", "arbitrary"),
            vmem_limit_bytes=48 * 1024 * 1024,
        ),
    )(info, q2, k, v, steer2)


def body(queries, keys_values, placement, lengths, steer_index, steering):
    shards = lax.axis_size("ctx")
    my_shard = lax.axis_index("ctx")
    tok_rows = queries.shape[0]
    half_rows = tok_rows // 2
    row_width = queries.shape[1]
    local_heads = row_width // HD
    local_kv = keys_values.shape[2] // HD
    group_size = local_heads // local_kv
    bit_count = shards.bit_length() - 1
    local_rows = jnp.arange(tok_rows, dtype=jnp.int32)
    first_half = local_rows < half_rows
    ends = jnp.cumsum(lengths).astype(jnp.int32)

    mask_rows = jnp.where(first_half, placement[0], placement[1])
    query_pos = jnp.bitwise_xor(my_shard, mask_rows) * tok_rows + local_rows
    qbase = jnp.bitwise_xor(my_shard, placement) * tok_rows + jnp.arange(2, dtype=jnp.int32) * half_rows
    qlast = qbase + half_rows - 1
    qs_first = request_start(qbase, ends)
    qs_last = request_start(qlast, ends)
    info = jnp.concatenate(
        [
            jnp.stack([qbase, qs_first // BK, qlast // BK, qs_last], axis=1).reshape(-1),
            ends,
        ]
    ).astype(jnp.int32)

    gathered = lax.all_gather(keys_values, "ctx", axis=0, tiled=True)
    g = gathered.reshape(shards, 2, half_rows, 2, HD)
    source = jnp.bitwise_xor(jnp.arange(shards, dtype=jnp.int32)[:, None], placement[None, :])
    packed = g[source, jnp.arange(2)[None, :]].reshape(shards * tok_rows, 2, HD)
    k = packed[:, 0]
    v = packed[:, 1]

    query_request = request_of(query_pos, lengths)
    chosen = steer_index[query_request]
    steer_rows = steering[chosen]

    q2 = queries.reshape(tok_rows * local_heads, HD)
    steer2 = steer_rows.reshape(tok_rows * local_heads, HD)
    out = attention(info, q2, k, v, steer2, group_size).reshape(tok_rows, row_width)

    for bit in range(bit_count):
        moved_out = partner(out, "ctx", bit)
        flags = jnp.right_shift(placement, bit) % 2
        out = jnp.where(
            (jnp.where(first_half, flags[0], flags[1]) == 1)[:, None], moved_out, out
        )
    return out


def solution(mesh):
    return jax.shard_map(
        body,
        mesh=mesh,
        in_specs=(P("ctx", "tp"), P("ctx", None, "tp"), P(), P(), P(), P(None, "tp")),
        out_specs=P("ctx", "tp"),
        check_vma=False,
    )
```

```python
import functools

import jax
import jax.numpy as jnp
from jax import lax
from jax.experimental import pallas as pl
from jax.experimental.pallas import tpu as pltpu
from jax.sharding import PartitionSpec as P

HD = 128
MOST = 10922
BK = 512
negative_fill = -1e30


def partner(value, axis, bit):
    mask = 2**bit
    pairs = [(source, source ^ mask) for source in range(lax.axis_size(axis))]
    return lax.ppermute(value, axis, pairs)


def request_of(positions, lengths):
    request_ends = jnp.cumsum(lengths)
    return jnp.sum((positions[:, None] >= request_ends[None, :]).astype(jnp.int32), axis=1)


def request_start(positions, ends):
    return jnp.max(jnp.where(ends[None, :] <= positions[:, None], ends[None, :], 0), axis=1)


def attention_kernel(group, steps, info_ref, q_ref, k0, k1, k2, k3, v0, v1, v2, v3, steer_ref, o_ref, m_sc, l_sc, acc_sc):
    j = pl.program_id(0)
    i = pl.program_id(1)
    rows = q_ref.shape[0]
    qbase = info_ref[j * 4 + 0]
    kstart = info_ref[j * 4 + 1]
    kend = info_ref[j * 4 + 2]
    qs_max = info_ref[j * 4 + 3]
    ends = [info_ref[8 + r] for r in range(8)]
    kb = kstart + i

    @pl.when(i == 0)
    def _():
        m_sc[...] = jnp.full(m_sc.shape, negative_fill, jnp.float32)
        l_sc[...] = jnp.zeros(l_sc.shape, jnp.float32)
        acc_sc[...] = jnp.zeros(acc_sc.shape, jnp.float32)

    def step(masked):
        q = q_ref[...]
        k = jnp.concatenate([k0[...], k1[...], k2[...], k3[...]], axis=0)
        v = jnp.concatenate([v0[...], v1[...], v2[...], v3[...]], axis=0)
        s = lax.dot_general(q, k, (((1,), (1,)), ((), ())), preferred_element_type=jnp.float32)
        s = s * (HD ** -0.5)
        if masked:
            qpos = qbase + lax.broadcasted_iota(jnp.int32, (rows, 1), 0) // group
            qstart = jnp.zeros((rows, 1), jnp.int32)
            for e in ends:
                qstart = jnp.where(e <= qpos, jnp.maximum(qstart, e), qstart)
            kpos = kb * BK + lax.broadcasted_iota(jnp.int32, (1, BK), 1)
            allowed = (kpos <= qpos) & (kpos >= qstart)
            s = jnp.where(allowed, s, negative_fill)
        m_old = m_sc[...]
        m_new = jnp.maximum(m_old, jnp.max(s, axis=1, keepdims=True))
        p = jnp.exp(s - m_new)
        if masked:
            p = jnp.where(allowed, p, 0.0)
        alpha = jnp.exp(m_old - m_new)
        l_sc[...] = alpha * l_sc[...] + jnp.sum(p, axis=1, keepdims=True)
        acc_sc[...] = alpha * acc_sc[...] + jnp.dot(
            p.astype(jnp.bfloat16), v, preferred_element_type=jnp.float32
        )
        m_sc[...] = m_new

    live = kb <= kend
    full = (kb * BK >= qs_max) & ((kb + 1) * BK - 1 <= qbase)

    @pl.when(live & full)
    def _():
        step(False)

    @pl.when(live & jnp.logical_not(full))
    def _():
        step(True)

    @pl.when(i == steps - 1)
    def _():
        attended = (acc_sc[...] / l_sc[...]).astype(jnp.bfloat16).astype(jnp.float32)
        o_ref[...] = (attended + steer_ref[...].astype(jnp.float32)).astype(o_ref.dtype)


def attention(info, q2, gathered, steer2, group):
    rows_all = q2.shape[0]
    half = rows_all // 2
    shards, _, tok_rows, _ = gathered.shape
    sub = tok_rows // 2
    per_step = BK // sub
    total_blocks = shards * tok_rows // BK
    steps = min(total_blocks, (MOST + half // group - 1) // BK + 2)

    def kv_spec(c, kv):
        def index_map(j, i, info_ref):
            kb = jnp.minimum(info_ref[j * 4 + 1] + i, info_ref[j * 4 + 2])
            b = kb * per_step + c
            return (jnp.bitwise_xor(b // 2, info_ref[16 + c % 2]), kv, c % 2, 0)

        return pl.BlockSpec((None, None, sub, HD), index_map)

    grid_spec = pltpu.PrefetchScalarGridSpec(
        num_scalar_prefetch=1,
        grid=(2, steps),
        in_specs=[
            pl.BlockSpec((half, HD), lambda j, i, info_ref: (j, 0)),
            *[kv_spec(c, 0) for c in range(per_step)],
            *[kv_spec(c, 1) for c in range(per_step)],
            pl.BlockSpec((half, HD), lambda j, i, info_ref: (j, 0)),
        ],
        out_specs=pl.BlockSpec((half, HD), lambda j, i, info_ref: (j, 0)),
        scratch_shapes=[
            pltpu.VMEM((half, 1), jnp.float32),
            pltpu.VMEM((half, 1), jnp.float32),
            pltpu.VMEM((half, HD), jnp.float32),
        ],
    )
    return pl.pallas_call(
        functools.partial(attention_kernel, group, steps),
        grid_spec=grid_spec,
        out_shape=jax.ShapeDtypeStruct((rows_all, HD), jnp.bfloat16),
        compiler_params=pltpu.CompilerParams(
            dimension_semantics=("arbitrary", "arbitrary"),
            vmem_limit_bytes=48 * 1024 * 1024,
        ),
    )(info, q2, *([gathered] * (2 * per_step)), steer2)


def body(queries, keys_values, placement, lengths, steer_index, steering):
    shards = lax.axis_size("ctx")
    my_shard = lax.axis_index("ctx")
    tok_rows = queries.shape[0]
    half_rows = tok_rows // 2
    row_width = queries.shape[1]
    local_heads = row_width // HD
    local_kv = keys_values.shape[2] // HD
    group_size = local_heads // local_kv
    bit_count = shards.bit_length() - 1
    local_rows = jnp.arange(tok_rows, dtype=jnp.int32)
    first_half = local_rows < half_rows
    ends = jnp.cumsum(lengths).astype(jnp.int32)

    mask_rows = jnp.where(first_half, placement[0], placement[1])
    query_pos = jnp.bitwise_xor(my_shard, mask_rows) * tok_rows + local_rows
    qbase = jnp.bitwise_xor(my_shard, placement) * tok_rows + jnp.arange(2, dtype=jnp.int32) * half_rows
    qlast = qbase + half_rows - 1
    qs_first = request_start(qbase, ends)
    qs_last = request_start(qlast, ends)
    info = jnp.concatenate(
        [
            jnp.stack([qbase, qs_first // BK, qlast // BK, qs_last], axis=1).reshape(-1),
            ends,
            placement,
        ]
    ).astype(jnp.int32)

    gathered = lax.all_gather(jnp.transpose(keys_values, (1, 0, 2)), "ctx", axis=0, tiled=False)

    query_request = request_of(query_pos, lengths)
    chosen = steer_index[query_request]
    one_hot = (chosen[:, None] == jnp.arange(steering.shape[0], dtype=jnp.int32)[None, :]).astype(
        jnp.bfloat16
    )
    steer_rows = jnp.dot(one_hot, steering, preferred_element_type=jnp.float32).astype(jnp.bfloat16)

    q2 = queries.reshape(tok_rows * local_heads, HD)
    steer2 = steer_rows.reshape(tok_rows * local_heads, HD)
    out = attention(info, q2, gathered, steer2, group_size).reshape(tok_rows, row_width)

    low_bits = bit_count // 2
    low_count = 1 << low_bits

    def move(piece, m):
        if m == 0:
            return piece
        return lax.ppermute(piece, "ctx", [(d, d ^ m) for d in range(shards)])

    def send(piece, mask):
        low = [functools.partial(move, m=m) for m in range(low_count)]
        high = [functools.partial(move, m=m * low_count) for m in range(shards // low_count)]
        piece = lax.switch(mask % low_count, low, piece)
        return lax.switch(mask // low_count, high, piece)

    halves = [send(out[j * half_rows:(j + 1) * half_rows], placement[j]) for j in range(2)]
    return jnp.concatenate(halves, axis=0)


def solution(mesh):
    return jax.shard_map(
        body,
        mesh=mesh,
        in_specs=(P("ctx", "tp"), P("ctx", None, "tp"), P(), P(), P(), P(None, "tp")),
        out_specs=P("ctx", "tp"),
        check_vma=False,
    )
```

```python
import functools

import jax
import jax.numpy as jnp
from jax import lax
from jax.experimental import pallas as pl
from jax.experimental.pallas import tpu as pltpu
from jax.sharding import PartitionSpec as P

HD = 128
MOST = 10922
negative_fill = -1e30


def partner(value, axis, bit):
    mask = 2**bit
    pairs = [(source, source ^ mask) for source in range(lax.axis_size(axis))]
    return lax.ppermute(value, axis, pairs)


def request_of(positions, lengths):
    request_ends = jnp.cumsum(lengths)
    return jnp.sum((positions[:, None] >= request_ends[None, :]).astype(jnp.int32), axis=1)


def request_start(positions, ends):
    return jnp.max(jnp.where(ends[None, :] <= positions[:, None], ends[None, :], 0), axis=1)


def attention_kernel(group, steps, key_half, first, last, info_ref, q_ref, *refs):
    k_refs, v_refs = refs[0:4], refs[4:8]
    refs = refs[8:]
    if last:
        steer_ref = refs[0]
        refs = refs[1:]
    if not first:
        m_in, l_in, acc_in = refs[0:3]
        refs = refs[3:]
    if last:
        o_ref = refs[0]
        refs = refs[1:]
    else:
        m_out, l_out, acc_out = refs[0:3]
        refs = refs[3:]
    m_sc, l_sc, acc_sc = refs
    j = pl.program_id(0)
    i = pl.program_id(1)
    rows = q_ref.shape[0]
    sub = k_refs[0].shape[0]
    width = len(k_refs) * sub
    span = len(k_refs) * 2 * sub
    qbase = info_ref[j * 4 + 0]
    kstart = info_ref[j * 4 + 1]
    kend = info_ref[j * 4 + 2]
    qs_max = info_ref[j * 4 + 3]
    ends = [info_ref[8 + r] for r in range(8)]
    kb = kstart + i

    @pl.when(i == 0)
    def _():
        if first:
            m_sc[...] = jnp.full(m_sc.shape, negative_fill, jnp.float32)
            l_sc[...] = jnp.zeros(l_sc.shape, jnp.float32)
            acc_sc[...] = jnp.zeros(acc_sc.shape, jnp.float32)
        else:
            m_sc[...] = m_in[...]
            l_sc[...] = l_in[...]
            acc_sc[...] = acc_in[...]

    def step(masked):
        q = q_ref[...]
        k = jnp.concatenate([r[...] for r in k_refs], axis=0)
        v = jnp.concatenate([r[...] for r in v_refs], axis=0)
        s = lax.dot_general(q, k, (((1,), (1,)), ((), ())), preferred_element_type=jnp.float32)
        s = s * (HD ** -0.5)
        if masked:
            qpos = qbase + lax.broadcasted_iota(jnp.int32, (rows, 1), 0) // group
            qstart = jnp.zeros((rows, 1), jnp.int32)
            for e in ends:
                qstart = jnp.where(e <= qpos, jnp.maximum(qstart, e), qstart)
            col = lax.broadcasted_iota(jnp.int32, (1, width), 1)
            kpos = kb * span + (col // sub) * (2 * sub) + key_half * sub + col % sub
            allowed = (kpos <= qpos) & (kpos >= qstart)
            s = jnp.where(allowed, s, negative_fill)
        m_old = m_sc[...]
        m_new = jnp.maximum(m_old, jnp.max(s, axis=1, keepdims=True))
        p = jnp.exp(s - m_new)
        if masked:
            p = jnp.where(allowed, p, 0.0)
        alpha = jnp.exp(m_old - m_new)
        l_sc[...] = alpha * l_sc[...] + jnp.sum(p, axis=1, keepdims=True)
        acc_sc[...] = alpha * acc_sc[...] + jnp.dot(
            p.astype(jnp.bfloat16), v, preferred_element_type=jnp.float32
        )
        m_sc[...] = m_new

    live = kb <= kend
    lo = kb * span + key_half * sub
    hi = kb * span + span - 2 * sub + key_half * sub + sub - 1
    full = (lo >= qs_max) & (hi <= qbase)

    @pl.when(live & full)
    def _():
        step(False)

    @pl.when(live & jnp.logical_not(full))
    def _():
        step(True)

    @pl.when(i == steps - 1)
    def _():
        if last:
            attended = (acc_sc[...] / l_sc[...]).astype(jnp.bfloat16).astype(jnp.float32)
            o_ref[...] = (attended + steer_ref[...].astype(jnp.float32)).astype(o_ref.dtype)
        else:
            m_out[...] = m_sc[...]
            l_out[...] = l_sc[...]
            acc_out[...] = acc_sc[...]


PER_STEP = 4


def attention_pass(info, q2, gathered, key_half, group, steer2=None, state=None):
    rows_all = q2.shape[0]
    half = rows_all // 2
    shards, _, sub, _ = gathered.shape
    span = PER_STEP * 2 * sub
    total_spans = shards * 2 * sub // span
    steps = min(total_spans, (MOST + half // group - 1) // span + 2)
    first = state is None
    last = steer2 is not None

    def kv_spec(c, kv):
        def index_map(j, i, info_ref):
            kb = jnp.minimum(info_ref[j * 4 + 1] + i, info_ref[j * 4 + 2])
            return (jnp.bitwise_xor(kb * PER_STEP + c, info_ref[16 + key_half]), kv, 0, 0)

        return pl.BlockSpec((None, None, sub, HD), index_map)

    row_spec = pl.BlockSpec((half, HD), lambda j, i, info_ref: (j, 0))
    col_spec = pl.BlockSpec((half, 1), lambda j, i, info_ref: (j, 0))
    in_specs = [row_spec] + [kv_spec(c, 0) for c in range(PER_STEP)] + [kv_spec(c, 1) for c in range(PER_STEP)]
    operands = [q2] + [gathered] * (2 * PER_STEP)
    if last:
        in_specs.append(row_spec)
        operands.append(steer2)
    if not first:
        in_specs += [col_spec, col_spec, row_spec]
        operands += list(state)
    if last:
        out_specs = row_spec
        out_shape = jax.ShapeDtypeStruct((rows_all, HD), jnp.bfloat16)
    else:
        out_specs = [col_spec, col_spec, row_spec]
        out_shape = [
            jax.ShapeDtypeStruct((rows_all, 1), jnp.float32),
            jax.ShapeDtypeStruct((rows_all, 1), jnp.float32),
            jax.ShapeDtypeStruct((rows_all, HD), jnp.float32),
        ]
    grid_spec = pltpu.PrefetchScalarGridSpec(
        num_scalar_prefetch=1,
        grid=(2, steps),
        in_specs=in_specs,
        out_specs=out_specs,
        scratch_shapes=[
            pltpu.VMEM((half, 1), jnp.float32),
            pltpu.VMEM((half, 1), jnp.float32),
            pltpu.VMEM((half, HD), jnp.float32),
        ],
    )
    return pl.pallas_call(
        functools.partial(attention_kernel, group, steps, key_half, first, last),
        grid_spec=grid_spec,
        out_shape=out_shape,
        compiler_params=pltpu.CompilerParams(
            dimension_semantics=("arbitrary", "arbitrary"),
            vmem_limit_bytes=48 * 1024 * 1024,
        ),
    )(info, *operands)


def body(queries, keys_values, placement, lengths, steer_index, steering):
    shards = lax.axis_size("ctx")
    my_shard = lax.axis_index("ctx")
    tok_rows = queries.shape[0]
    half_rows = tok_rows // 2
    row_width = queries.shape[1]
    local_heads = row_width // HD
    local_kv = keys_values.shape[2] // HD
    group_size = local_heads // local_kv
    bit_count = shards.bit_length() - 1
    local_rows = jnp.arange(tok_rows, dtype=jnp.int32)
    first_half = local_rows < half_rows
    ends = jnp.cumsum(lengths).astype(jnp.int32)

    mask_rows = jnp.where(first_half, placement[0], placement[1])
    query_pos = jnp.bitwise_xor(my_shard, mask_rows) * tok_rows + local_rows
    qbase = jnp.bitwise_xor(my_shard, placement) * tok_rows + jnp.arange(2, dtype=jnp.int32) * half_rows
    qlast = qbase + half_rows - 1
    span = PER_STEP * tok_rows
    qs_first = request_start(qbase, ends)
    qs_last = request_start(qlast, ends)
    info = jnp.concatenate(
        [
            jnp.stack([qbase, qs_first // span, qlast // span, qs_last], axis=1).reshape(-1),
            ends,
            placement,
        ]
    ).astype(jnp.int32)

    kv_t = jnp.transpose(keys_values, (1, 0, 2))
    gathered = [
        lax.all_gather(kv_t[:, j * half_rows:(j + 1) * half_rows], "ctx", axis=0, tiled=False)
        for j in range(2)
    ]

    query_request = request_of(query_pos, lengths)
    chosen = steer_index[query_request]
    one_hot = (chosen[:, None] == jnp.arange(steering.shape[0], dtype=jnp.int32)[None, :]).astype(
        jnp.bfloat16
    )
    steer_rows = jnp.dot(one_hot, steering, preferred_element_type=jnp.float32).astype(jnp.bfloat16)

    q2 = queries.reshape(tok_rows * local_heads, HD)
    steer2 = steer_rows.reshape(tok_rows * local_heads, HD)
    state = attention_pass(info, q2, gathered[0], 0, group_size)
    out = attention_pass(info, q2, gathered[1], 1, group_size, steer2=steer2, state=state)
    out = out.reshape(tok_rows, row_width)

    low_bits = bit_count // 2
    low_count = 1 << low_bits

    def move(piece, m):
        if m == 0:
            return piece
        return lax.ppermute(piece, "ctx", [(d, d ^ m) for d in range(shards)])

    def send(piece, mask):
        low = [functools.partial(move, m=m) for m in range(low_count)]
        high = [functools.partial(move, m=m * low_count) for m in range(shards // low_count)]
        piece = lax.switch(mask % low_count, low, piece)
        return lax.switch(mask // low_count, high, piece)

    halves = [send(out[j * half_rows:(j + 1) * half_rows], placement[j]) for j in range(2)]
    return jnp.concatenate(halves, axis=0)


def solution(mesh):
    return jax.shard_map(
        body,
        mesh=mesh,
        in_specs=(P("ctx", "tp"), P("ctx", None, "tp"), P(), P(), P(), P(None, "tp")),
        out_specs=P("ctx", "tp"),
        check_vma=False,
    )
```

```python
import functools

import jax
import jax.numpy as jnp
from jax import lax
from jax.experimental import pallas as pl
from jax.experimental.pallas import tpu as pltpu
from jax.sharding import PartitionSpec as P

HD = 128
MOST = 10922
BK = 512
negative_fill = -1e30


def partner(value, axis, bit):
    mask = 2**bit
    pairs = [(source, source ^ mask) for source in range(lax.axis_size(axis))]
    return lax.ppermute(value, axis, pairs)


def request_of(positions, lengths):
    request_ends = jnp.cumsum(lengths)
    return jnp.sum((positions[:, None] >= request_ends[None, :]).astype(jnp.int32), axis=1)


def request_start(positions, ends):
    return jnp.max(jnp.where(ends[None, :] <= positions[:, None], ends[None, :], 0), axis=1)


def attention_kernel(group, steps, info_ref, q_ref, k0, k1, k2, k3, v0, v1, v2, v3, steer_ref, o_ref, m_sc, l_sc, acc_sc):
    j = pl.program_id(0)
    i = pl.program_id(1)
    rows = q_ref.shape[0]
    qbase = info_ref[j * 4 + 0]
    kstart = info_ref[j * 4 + 1]
    kend = info_ref[j * 4 + 2]
    qs_max = info_ref[j * 4 + 3]
    ends = [info_ref[8 + r] for r in range(8)]
    kb = kstart + i

    @pl.when(i == 0)
    def _():
        m_sc[...] = jnp.full(m_sc.shape, negative_fill, jnp.float32)
        l_sc[...] = jnp.zeros(l_sc.shape, jnp.float32)
        acc_sc[...] = jnp.zeros(acc_sc.shape, jnp.float32)

    def step(masked):
        q = q_ref[...]
        k = jnp.concatenate([k0[...], k1[...], k2[...], k3[...]], axis=0)
        v = jnp.concatenate([v0[...], v1[...], v2[...], v3[...]], axis=0)
        s = lax.dot_general(q, k, (((1,), (1,)), ((), ())), preferred_element_type=jnp.float32)
        s = s * (HD ** -0.5)
        if masked:
            qpos = qbase + lax.broadcasted_iota(jnp.int32, (rows, 1), 0) // group
            qstart = jnp.zeros((rows, 1), jnp.int32)
            for e in ends:
                qstart = jnp.where(e <= qpos, jnp.maximum(qstart, e), qstart)
            kpos = kb * BK + lax.broadcasted_iota(jnp.int32, (1, BK), 1)
            allowed = (kpos <= qpos) & (kpos >= qstart)
            s = jnp.where(allowed, s, negative_fill)
        m_old = m_sc[...]
        m_new = jnp.maximum(m_old, jnp.max(s, axis=1, keepdims=True))
        p = jnp.exp(s - m_new)
        if masked:
            p = jnp.where(allowed, p, 0.0)
        alpha = jnp.exp(m_old - m_new)
        l_sc[...] = alpha * l_sc[...] + jnp.sum(p, axis=1, keepdims=True)
        acc_sc[...] = alpha * acc_sc[...] + jnp.dot(
            p.astype(jnp.bfloat16), v, preferred_element_type=jnp.float32
        )
        m_sc[...] = m_new

    live = kb <= kend
    full = (kb * BK >= qs_max) & ((kb + 1) * BK - 1 <= qbase)

    @pl.when(live & full)
    def _():
        step(False)

    @pl.when(live & jnp.logical_not(full))
    def _():
        step(True)

    @pl.when(i == steps - 1)
    def _():
        attended = (acc_sc[...] / l_sc[...]).astype(jnp.bfloat16).astype(jnp.float32)
        o_ref[...] = (attended + steer_ref[...].astype(jnp.float32)).astype(o_ref.dtype)


def attention(info, q2, gathered, steer2, group):
    rows_all = q2.shape[0]
    half = rows_all // 2
    shards, _, tok_rows, _ = gathered.shape
    sub = tok_rows // 2
    per_step = BK // sub
    total_blocks = shards * tok_rows // BK
    steps = min(total_blocks, (MOST + half // group - 1) // BK + 2)

    def kv_spec(c, kv):
        def index_map(j, i, info_ref):
            kb = jnp.minimum(info_ref[j * 4 + 1] + i, info_ref[j * 4 + 2])
            b = kb * per_step + c
            return (jnp.bitwise_xor(b // 2, info_ref[16 + c % 2]), kv, c % 2, 0)

        return pl.BlockSpec((None, None, sub, HD), index_map)

    grid_spec = pltpu.PrefetchScalarGridSpec(
        num_scalar_prefetch=1,
        grid=(2, steps),
        in_specs=[
            pl.BlockSpec((half, HD), lambda j, i, info_ref: (j, 0)),
            *[kv_spec(c, 0) for c in range(per_step)],
            *[kv_spec(c, 1) for c in range(per_step)],
            pl.BlockSpec((half, HD), lambda j, i, info_ref: (j, 0)),
        ],
        out_specs=pl.BlockSpec((half, HD), lambda j, i, info_ref: (j, 0)),
        scratch_shapes=[
            pltpu.VMEM((half, 1), jnp.float32),
            pltpu.VMEM((half, 1), jnp.float32),
            pltpu.VMEM((half, HD), jnp.float32),
        ],
    )
    return pl.pallas_call(
        functools.partial(attention_kernel, group, steps),
        grid_spec=grid_spec,
        out_shape=jax.ShapeDtypeStruct((rows_all, HD), jnp.bfloat16),
        compiler_params=pltpu.CompilerParams(
            dimension_semantics=("arbitrary", "arbitrary"),
            vmem_limit_bytes=48 * 1024 * 1024,
        ),
    )(info, q2, *([gathered] * (2 * per_step)), steer2)


def body(queries, keys_values, placement, lengths, steer_index, steering):
    shards = lax.axis_size("ctx")
    my_shard = lax.axis_index("ctx")
    tok_rows = queries.shape[0]
    half_rows = tok_rows // 2
    row_width = queries.shape[1]
    local_heads = row_width // HD
    local_kv = keys_values.shape[2] // HD
    group_size = local_heads // local_kv
    bit_count = shards.bit_length() - 1
    local_rows = jnp.arange(tok_rows, dtype=jnp.int32)
    first_half = local_rows < half_rows
    ends = jnp.cumsum(lengths).astype(jnp.int32)

    low_bits = bit_count // 2
    low_count = 1 << low_bits

    def move(piece, m):
        if m == 0:
            return piece
        return lax.ppermute(piece, "ctx", [(d, d ^ m) for d in range(shards)])

    def send(piece, mask):
        low = [functools.partial(move, m=m) for m in range(low_count)]
        high = [functools.partial(move, m=m * low_count) for m in range(shards // low_count)]
        piece = lax.switch(mask % low_count, low, piece)
        return lax.switch(mask // low_count, high, piece)

    queries = jnp.concatenate(
        [send(queries[j * half_rows:(j + 1) * half_rows], placement[j]) for j in range(2)], axis=0
    )
    query_pos = my_shard * tok_rows + local_rows
    qbase = my_shard * tok_rows + jnp.arange(2, dtype=jnp.int32) * half_rows
    qlast = qbase + half_rows - 1
    qs_first = request_start(qbase, ends)
    qs_last = request_start(qlast, ends)
    info = jnp.concatenate(
        [
            jnp.stack([qbase, qs_first // BK, qlast // BK, qs_last], axis=1).reshape(-1),
            ends,
            placement,
        ]
    ).astype(jnp.int32)

    gathered = lax.all_gather(jnp.transpose(keys_values, (1, 0, 2)), "ctx", axis=0, tiled=False)

    query_request = request_of(query_pos, lengths)
    chosen = steer_index[query_request]
    one_hot = (chosen[:, None] == jnp.arange(steering.shape[0], dtype=jnp.int32)[None, :]).astype(
        jnp.bfloat16
    )
    steer_rows = jnp.dot(one_hot, steering, preferred_element_type=jnp.float32).astype(jnp.bfloat16)

    q2 = queries.reshape(tok_rows * local_heads, HD)
    steer2 = steer_rows.reshape(tok_rows * local_heads, HD)
    out = attention(info, q2, gathered, steer2, group_size).reshape(tok_rows, row_width)

    return out


def solution(mesh):
    return jax.shard_map(
        body,
        mesh=mesh,
        in_specs=(P("ctx", "tp"), P("ctx", None, "tp"), P(), P(), P(), P(None, "tp")),
        out_specs=P("ctx", "tp"),
        check_vma=False,
    )
```

```python
import functools

import jax
import jax.numpy as jnp
from jax import lax
from jax.experimental import pallas as pl
from jax.experimental.pallas import tpu as pltpu
from jax.sharding import PartitionSpec as P

HD = 128
MOST = 10922
BK = 256
negative_fill = -1e30


def partner(value, axis, bit):
    mask = 2**bit
    pairs = [(source, source ^ mask) for source in range(lax.axis_size(axis))]
    return lax.ppermute(value, axis, pairs)


def request_of(positions, lengths):
    request_ends = jnp.cumsum(lengths)
    return jnp.sum((positions[:, None] >= request_ends[None, :]).astype(jnp.int32), axis=1)


def request_start(positions, ends):
    return jnp.max(jnp.where(ends[None, :] <= positions[:, None], ends[None, :], 0), axis=1)


def attention_kernel(group, steps, info_ref, q_ref, *refs):
    per_step = (len(refs) - 5) // 2
    k_refs, v_refs = refs[:per_step], refs[per_step:2 * per_step]
    steer_ref, o_ref, m_sc, l_sc, acc_sc = refs[2 * per_step:]
    j = pl.program_id(0)
    i = pl.program_id(1)
    rows = q_ref.shape[0]
    qbase = info_ref[j * 4 + 0]
    kstart = info_ref[j * 4 + 1]
    kend = info_ref[j * 4 + 2]
    qs_max = info_ref[j * 4 + 3]
    ends = [info_ref[8 + r] for r in range(8)]
    kb = kstart + i

    @pl.when(i == 0)
    def _():
        m_sc[...] = jnp.full(m_sc.shape, negative_fill, jnp.float32)
        l_sc[...] = jnp.zeros(l_sc.shape, jnp.float32)
        acc_sc[...] = jnp.zeros(acc_sc.shape, jnp.float32)

    def step(masked):
        q = q_ref[...]
        k = jnp.concatenate([r[...] for r in k_refs], axis=0)
        v = jnp.concatenate([r[...] for r in v_refs], axis=0)
        s = lax.dot_general(q, k, (((1,), (1,)), ((), ())), preferred_element_type=jnp.float32)
        if masked:
            qpos = qbase + lax.broadcasted_iota(jnp.int32, (rows, 1), 0) // group
            qstart = jnp.zeros((rows, 1), jnp.int32)
            for e in ends:
                qstart = jnp.where(e <= qpos, jnp.maximum(qstart, e), qstart)
            kpos = kb * BK + lax.broadcasted_iota(jnp.int32, (1, BK), 1)
            allowed = (kpos <= qpos) & (kpos >= qstart)
            s = jnp.where(allowed, s, negative_fill)
        m_old = m_sc[...]
        reps = s.shape[1] // m_old.shape[1]
        m_new = jnp.maximum(m_old, jnp.max(s, axis=1, keepdims=True))
        p = jnp.exp((s - jnp.tile(m_new, (1, reps))) * (HD ** -0.5))
        if masked:
            p = jnp.where(allowed, p, 0.0)
        alpha = jnp.exp((m_old - m_new) * (HD ** -0.5))
        l_sc[...] = alpha * l_sc[...] + jnp.sum(p, axis=1, keepdims=True)
        acc_sc[...] = alpha * acc_sc[...] + jnp.dot(
            p.astype(jnp.bfloat16), v, preferred_element_type=jnp.float32
        )
        m_sc[...] = m_new

    live = kb <= kend
    full = (kb * BK >= qs_max) & ((kb + 1) * BK - 1 <= qbase)

    @pl.when(live & full)
    def _():
        step(False)

    @pl.when(live & jnp.logical_not(full))
    def _():
        step(True)

    @pl.when(i == steps - 1)
    def _():
        attended = (acc_sc[...] / l_sc[...]).astype(jnp.bfloat16).astype(jnp.float32)
        o_ref[...] = (attended + steer_ref[...].astype(jnp.float32)).astype(o_ref.dtype)


def attention(info, q2, gathered, steer2, group):
    rows_all = q2.shape[0]
    half = rows_all // 2
    shards, _, tok_rows, _ = gathered.shape
    sub = tok_rows // 2
    per_step = BK // sub
    total_blocks = shards * tok_rows // BK
    steps = min(total_blocks, (MOST + half // group - 1) // BK + 2)

    def kv_spec(c, kv):
        def index_map(j, i, info_ref):
            kb = jnp.minimum(info_ref[j * 4 + 1] + i, info_ref[j * 4 + 2])
            b = kb * per_step + c
            return (jnp.bitwise_xor(b // 2, info_ref[16 + c % 2]), kv, c % 2, 0)

        return pl.BlockSpec((None, None, sub, HD), index_map)

    grid_spec = pltpu.PrefetchScalarGridSpec(
        num_scalar_prefetch=1,
        grid=(2, steps),
        in_specs=[
            pl.BlockSpec((half, HD), lambda j, i, info_ref: (j, 0)),
            *[kv_spec(c, 0) for c in range(per_step)],
            *[kv_spec(c, 1) for c in range(per_step)],
            pl.BlockSpec((half, HD), lambda j, i, info_ref: (j, 0)),
        ],
        out_specs=pl.BlockSpec((half, HD), lambda j, i, info_ref: (j, 0)),
        scratch_shapes=[
            pltpu.VMEM((half, HD), jnp.float32),
            pltpu.VMEM((half, HD), jnp.float32),
            pltpu.VMEM((half, HD), jnp.float32),
        ],
    )
    return pl.pallas_call(
        functools.partial(attention_kernel, group, steps),
        grid_spec=grid_spec,
        out_shape=jax.ShapeDtypeStruct((rows_all, HD), jnp.bfloat16),
        compiler_params=pltpu.CompilerParams(
            dimension_semantics=("arbitrary", "arbitrary"),
            vmem_limit_bytes=48 * 1024 * 1024,
        ),
    )(info, q2, *([gathered] * (2 * per_step)), steer2)


def body(queries, keys_values, placement, lengths, steer_index, steering):
    shards = lax.axis_size("ctx")
    my_shard = lax.axis_index("ctx")
    tok_rows = queries.shape[0]
    half_rows = tok_rows // 2
    row_width = queries.shape[1]
    local_heads = row_width // HD
    local_kv = keys_values.shape[2] // HD
    group_size = local_heads // local_kv
    bit_count = shards.bit_length() - 1
    local_rows = jnp.arange(tok_rows, dtype=jnp.int32)
    first_half = local_rows < half_rows
    ends = jnp.cumsum(lengths).astype(jnp.int32)

    mask_rows = jnp.where(first_half, placement[0], placement[1])
    query_pos = jnp.bitwise_xor(my_shard, mask_rows) * tok_rows + local_rows
    qbase = jnp.bitwise_xor(my_shard, placement) * tok_rows + jnp.arange(2, dtype=jnp.int32) * half_rows
    qlast = qbase + half_rows - 1
    qs_first = request_start(qbase, ends)
    qs_last = request_start(qlast, ends)
    info = jnp.concatenate(
        [
            jnp.stack([qbase, qs_first // BK, qlast // BK, qs_last], axis=1).reshape(-1),
            ends,
            placement,
        ]
    ).astype(jnp.int32)

    gathered = lax.all_gather(jnp.transpose(keys_values, (1, 0, 2)), "ctx", axis=0, tiled=False)

    query_request = request_of(query_pos, lengths)
    chosen = steer_index[query_request]
    one_hot = (chosen[:, None] == jnp.arange(steering.shape[0], dtype=jnp.int32)[None, :]).astype(
        jnp.bfloat16
    )
    steer_rows = jnp.dot(one_hot, steering, preferred_element_type=jnp.float32).astype(jnp.bfloat16)

    q2 = queries.reshape(tok_rows * local_heads, HD)
    steer2 = steer_rows.reshape(tok_rows * local_heads, HD)
    out = attention(info, q2, gathered, steer2, group_size).reshape(tok_rows, row_width)

    low_bits = bit_count // 2
    low_count = 1 << low_bits

    def move(piece, m):
        if m == 0:
            return piece
        return lax.ppermute(piece, "ctx", [(d, d ^ m) for d in range(shards)])

    def send(piece, mask):
        low = [functools.partial(move, m=m) for m in range(low_count)]
        high = [functools.partial(move, m=m * low_count) for m in range(shards // low_count)]
        piece = lax.switch(mask % low_count, low, piece)
        return lax.switch(mask // low_count, high, piece)

    halves = [send(out[j * half_rows:(j + 1) * half_rows], placement[j]) for j in range(2)]
    return jnp.concatenate(halves, axis=0)


def solution(mesh):
    return jax.shard_map(
        body,
        mesh=mesh,
        in_specs=(P("ctx", "tp"), P("ctx", None, "tp"), P(), P(), P(), P(None, "tp")),
        out_specs=P("ctx", "tp"),
        check_vma=False,
    )
```

```python
import functools

import jax
import jax.numpy as jnp
from jax import lax
from jax.experimental import pallas as pl
from jax.experimental.pallas import tpu as pltpu
from jax.sharding import PartitionSpec as P

HD = 128
MOST = 10922
BK = 512
negative_fill = -1e30


def partner(value, axis, bit):
    mask = 2**bit
    pairs = [(source, source ^ mask) for source in range(lax.axis_size(axis))]
    return lax.ppermute(value, axis, pairs)


def request_of(positions, lengths):
    request_ends = jnp.cumsum(lengths)
    return jnp.sum((positions[:, None] >= request_ends[None, :]).astype(jnp.int32), axis=1)


def request_start(positions, ends):
    return jnp.max(jnp.where(ends[None, :] <= positions[:, None], ends[None, :], 0), axis=1)


def attention_kernel(group, steps, info_ref, q_ref, *refs):
    per_step = (len(refs) - 7) // 2
    k_refs, v_refs = refs[:per_step], refs[per_step:2 * per_step]
    steer_ref, o_ref, m_sc, l_sc, acc_sc, qpos_sc, qstart_sc = refs[2 * per_step:]
    j = pl.program_id(0)
    i = pl.program_id(1)
    rows = q_ref.shape[0]
    qbase = info_ref[j * 4 + 0]
    kstart = info_ref[j * 4 + 1]
    kend = info_ref[j * 4 + 2]
    qs_max = info_ref[j * 4 + 3]
    ends = [info_ref[8 + r] for r in range(8)]
    kb = kstart + i

    @pl.when(i == 0)
    def _():
        m_sc[...] = jnp.full(m_sc.shape, negative_fill, jnp.float32)
        l_sc[...] = jnp.zeros(l_sc.shape, jnp.float32)
        acc_sc[...] = jnp.zeros(acc_sc.shape, jnp.float32)
        qpos = qbase + lax.broadcasted_iota(jnp.int32, qpos_sc.shape, 0) // group
        qstart = jnp.zeros(qpos_sc.shape, jnp.int32)
        for e in ends:
            qstart = jnp.where(e <= qpos, jnp.maximum(qstart, e), qstart)
        qpos_sc[...] = qpos
        qstart_sc[...] = qstart

    def step(masked):
        q = q_ref[...]
        k = jnp.concatenate([r[...] for r in k_refs], axis=0)
        v = jnp.concatenate([r[...] for r in v_refs], axis=0)
        s = lax.dot_general(q, k, (((1,), (1,)), ((), ())), preferred_element_type=jnp.float32)
        if masked:
            reps = BK // qpos_sc.shape[1]
            qpos = jnp.tile(qpos_sc[...], (1, reps))
            qstart = jnp.tile(qstart_sc[...], (1, reps))
            kpos = kb * BK + lax.broadcasted_iota(jnp.int32, (1, BK), 1)
            allowed = (kpos <= qpos) & (kpos >= qstart)
            s = jnp.where(allowed, s, negative_fill)
        m_old = m_sc[...]
        reps = s.shape[1] // m_old.shape[1]
        m_new = jnp.maximum(m_old, jnp.max(s, axis=1, keepdims=True))
        p = jnp.exp((s - jnp.tile(m_new, (1, reps))) * (HD ** -0.5))
        if masked:
            p = jnp.where(allowed, p, 0.0)
        alpha = jnp.exp((m_old - m_new) * (HD ** -0.5))
        l_sc[...] = alpha * l_sc[...] + jnp.sum(p, axis=1, keepdims=True)
        acc_sc[...] = alpha * acc_sc[...] + jnp.dot(
            p.astype(jnp.bfloat16), v, preferred_element_type=jnp.float32
        )
        m_sc[...] = m_new

    live = kb <= kend
    full = (kb * BK >= qs_max) & ((kb + 1) * BK - 1 <= qbase)

    @pl.when(live & full)
    def _():
        step(False)

    @pl.when(live & jnp.logical_not(full))
    def _():
        step(True)

    @pl.when(i == steps - 1)
    def _():
        attended = (acc_sc[...] / l_sc[...]).astype(jnp.bfloat16).astype(jnp.float32)
        o_ref[...] = (attended + steer_ref[...].astype(jnp.float32)).astype(o_ref.dtype)


def attention(info, q2, gathered, steer2, group):
    rows_all = q2.shape[0]
    half = rows_all // 2
    shards, _, tok_rows, _ = gathered.shape
    sub = tok_rows // 2
    per_step = BK // sub
    total_blocks = shards * tok_rows // BK
    steps = min(total_blocks, (MOST + half // group - 1) // BK + 2)

    def kv_spec(c, kv):
        def index_map(j, i, info_ref):
            kb = jnp.minimum(info_ref[j * 4 + 1] + i, info_ref[j * 4 + 2])
            b = kb * per_step + c
            return (jnp.bitwise_xor(b // 2, info_ref[16 + c % 2]), kv, c % 2, 0)

        return pl.BlockSpec((None, None, sub, HD), index_map)

    grid_spec = pltpu.PrefetchScalarGridSpec(
        num_scalar_prefetch=1,
        grid=(2, steps),
        in_specs=[
            pl.BlockSpec((half, HD), lambda j, i, info_ref: (j, 0)),
            *[kv_spec(c, 0) for c in range(per_step)],
            *[kv_spec(c, 1) for c in range(per_step)],
            pl.BlockSpec((half, HD), lambda j, i, info_ref: (j, 0)),
        ],
        out_specs=pl.BlockSpec((half, HD), lambda j, i, info_ref: (j, 0)),
        scratch_shapes=[
            pltpu.VMEM((half, HD), jnp.float32),
            pltpu.VMEM((half, HD), jnp.float32),
            pltpu.VMEM((half, HD), jnp.float32),
            pltpu.VMEM((half, HD), jnp.int32),
            pltpu.VMEM((half, HD), jnp.int32),
        ],
    )
    return pl.pallas_call(
        functools.partial(attention_kernel, group, steps),
        grid_spec=grid_spec,
        out_shape=jax.ShapeDtypeStruct((rows_all, HD), jnp.bfloat16),
        compiler_params=pltpu.CompilerParams(
            dimension_semantics=("arbitrary", "arbitrary"),
            vmem_limit_bytes=48 * 1024 * 1024,
        ),
    )(info, q2, *([gathered] * (2 * per_step)), steer2)


def body(queries, keys_values, placement, lengths, steer_index, steering):
    shards = lax.axis_size("ctx")
    my_shard = lax.axis_index("ctx")
    tok_rows = queries.shape[0]
    half_rows = tok_rows // 2
    row_width = queries.shape[1]
    local_heads = row_width // HD
    local_kv = keys_values.shape[2] // HD
    group_size = local_heads // local_kv
    bit_count = shards.bit_length() - 1
    local_rows = jnp.arange(tok_rows, dtype=jnp.int32)
    first_half = local_rows < half_rows
    ends = jnp.cumsum(lengths).astype(jnp.int32)

    mask_rows = jnp.where(first_half, placement[0], placement[1])
    query_pos = jnp.bitwise_xor(my_shard, mask_rows) * tok_rows + local_rows
    qbase = jnp.bitwise_xor(my_shard, placement) * tok_rows + jnp.arange(2, dtype=jnp.int32) * half_rows
    qlast = qbase + half_rows - 1
    qs_first = request_start(qbase, ends)
    qs_last = request_start(qlast, ends)
    info = jnp.concatenate(
        [
            jnp.stack([qbase, qs_first // BK, qlast // BK, qs_last], axis=1).reshape(-1),
            ends,
            placement,
        ]
    ).astype(jnp.int32)

    gathered = lax.all_gather(jnp.transpose(keys_values, (1, 0, 2)), "ctx", axis=0, tiled=False)

    query_request = request_of(query_pos, lengths)
    chosen = steer_index[query_request]
    one_hot = (chosen[:, None] == jnp.arange(steering.shape[0], dtype=jnp.int32)[None, :]).astype(
        jnp.bfloat16
    )
    steer_rows = jnp.dot(one_hot, steering, preferred_element_type=jnp.float32).astype(jnp.bfloat16)

    q2 = queries.reshape(tok_rows * local_heads, HD)
    steer2 = steer_rows.reshape(tok_rows * local_heads, HD)
    out = attention(info, q2, gathered, steer2, group_size).reshape(tok_rows, row_width)

    low_bits = bit_count // 2
    low_count = 1 << low_bits

    def move(piece, m):
        if m == 0:
            return piece
        return lax.ppermute(piece, "ctx", [(d, d ^ m) for d in range(shards)])

    def send(piece, mask):
        low = [functools.partial(move, m=m) for m in range(low_count)]
        high = [functools.partial(move, m=m * low_count) for m in range(shards // low_count)]
        piece = lax.switch(mask % low_count, low, piece)
        return lax.switch(mask // low_count, high, piece)

    halves = [send(out[j * half_rows:(j + 1) * half_rows], placement[j]) for j in range(2)]
    return jnp.concatenate(halves, axis=0)


def solution(mesh):
    return jax.shard_map(
        body,
        mesh=mesh,
        in_specs=(P("ctx", "tp"), P("ctx", None, "tp"), P(), P(), P(), P(None, "tp")),
        out_specs=P("ctx", "tp"),
        check_vma=False,
    )
```

```python
import functools
import math

import jax
import jax.numpy as jnp
from jax import lax
from jax.experimental import pallas as pl
from jax.experimental.pallas import tpu as pltpu
from jax.sharding import PartitionSpec as P

HD = 128
MOST = 10922
BK = 512
negative_fill = -1e30
EXP2_SCALE = math.log2(math.e) / math.sqrt(HD)


def partner(value, axis, bit):
    mask = 2**bit
    pairs = [(source, source ^ mask) for source in range(lax.axis_size(axis))]
    return lax.ppermute(value, axis, pairs)


def request_of(positions, lengths):
    request_ends = jnp.cumsum(lengths)
    return jnp.sum((positions[:, None] >= request_ends[None, :]).astype(jnp.int32), axis=1)


def request_start(positions, ends):
    return jnp.max(jnp.where(ends[None, :] <= positions[:, None], ends[None, :], 0), axis=1)


def attention_kernel(group, steps, info_ref, q_ref, *refs):
    per_step = (len(refs) - 7) // 2
    k_refs, v_refs = refs[:per_step], refs[per_step:2 * per_step]
    steer_ref, o_ref, m_sc, l_sc, acc_sc, qpos_sc, qstart_sc = refs[2 * per_step:]
    j = pl.program_id(0)
    i = pl.program_id(1)
    rows = q_ref.shape[0]
    qbase = info_ref[j * 4 + 0]
    kstart = info_ref[j * 4 + 1]
    kend = info_ref[j * 4 + 2]
    qs_max = info_ref[j * 4 + 3]
    ends = [info_ref[8 + r] for r in range(8)]
    kb = kstart + i

    @pl.when(i == 0)
    def _():
        m_sc[...] = jnp.full(m_sc.shape, negative_fill, jnp.float32)
        l_sc[...] = jnp.zeros(l_sc.shape, jnp.float32)
        acc_sc[...] = jnp.zeros(acc_sc.shape, jnp.float32)
        qpos = qbase + lax.broadcasted_iota(jnp.int32, qpos_sc.shape, 0) // group
        qstart = jnp.zeros(qpos_sc.shape, jnp.int32)
        for e in ends:
            qstart = jnp.where(e <= qpos, jnp.maximum(qstart, e), qstart)
        qpos_sc[...] = qpos
        qstart_sc[...] = qstart

    def step(masked):
        q = q_ref[...]
        k = jnp.concatenate([r[...] for r in k_refs], axis=0)
        v = jnp.concatenate([r[...] for r in v_refs], axis=0)
        s = lax.dot_general(q, k, (((1,), (1,)), ((), ())), preferred_element_type=jnp.float32)
        if masked:
            reps = BK // qpos_sc.shape[1]
            qpos = jnp.tile(qpos_sc[...], (1, reps))
            qstart = jnp.tile(qstart_sc[...], (1, reps))
            kpos = kb * BK + lax.broadcasted_iota(jnp.int32, (1, BK), 1)
            allowed = (kpos <= qpos) & (kpos >= qstart)
            s = jnp.where(allowed, s, negative_fill)
        m_old = m_sc[...]
        reps = s.shape[1] // m_old.shape[1]
        m_new = jnp.maximum(m_old, jnp.max(s, axis=1, keepdims=True))
        p = jnp.exp2((s - jnp.tile(m_new, (1, reps))) * EXP2_SCALE)
        if masked:
            p = jnp.where(allowed, p, 0.0)
        alpha = jnp.exp2((m_old - m_new) * EXP2_SCALE)
        l_sc[...] = alpha * l_sc[...] + jnp.sum(p, axis=1, keepdims=True)
        acc_sc[...] = alpha * acc_sc[...] + jnp.dot(
            p.astype(jnp.bfloat16), v, preferred_element_type=jnp.float32
        )
        m_sc[...] = m_new

    live = kb <= kend
    full = (kb * BK >= qs_max) & ((kb + 1) * BK - 1 <= qbase)

    @pl.when(live & full)
    def _():
        step(False)

    @pl.when(live & jnp.logical_not(full))
    def _():
        step(True)

    @pl.when(i == steps - 1)
    def _():
        attended = (acc_sc[...] / l_sc[...]).astype(jnp.bfloat16).astype(jnp.float32)
        o_ref[...] = (attended + steer_ref[...].astype(jnp.float32)).astype(o_ref.dtype)


def attention(info, q2, gathered, steer2, group):
    rows_all = q2.shape[0]
    half = rows_all // 2
    shards, _, tok_rows, _ = gathered.shape
    sub = tok_rows // 2
    per_step = BK // sub
    total_blocks = shards * tok_rows // BK
    steps = min(total_blocks, (MOST + half // group - 1) // BK + 2)

    def kv_spec(c, kv):
        def index_map(j, i, info_ref):
            kb = jnp.minimum(info_ref[j * 4 + 1] + i, info_ref[j * 4 + 2])
            b = kb * per_step + c
            return (jnp.bitwise_xor(b // 2, info_ref[16 + c % 2]), kv, c % 2, 0)

        return pl.BlockSpec((None, None, sub, HD), index_map)

    grid_spec = pltpu.PrefetchScalarGridSpec(
        num_scalar_prefetch=1,
        grid=(2, steps),
        in_specs=[
            pl.BlockSpec((half, HD), lambda j, i, info_ref: (j, 0)),
            *[kv_spec(c, 0) for c in range(per_step)],
            *[kv_spec(c, 1) for c in range(per_step)],
            pl.BlockSpec((half, HD), lambda j, i, info_ref: (j, 0)),
        ],
        out_specs=pl.BlockSpec((half, HD), lambda j, i, info_ref: (j, 0)),
        scratch_shapes=[
            pltpu.VMEM((half, HD), jnp.float32),
            pltpu.VMEM((half, HD), jnp.float32),
            pltpu.VMEM((half, HD), jnp.float32),
            pltpu.VMEM((half, HD), jnp.int32),
            pltpu.VMEM((half, HD), jnp.int32),
        ],
    )
    return pl.pallas_call(
        functools.partial(attention_kernel, group, steps),
        grid_spec=grid_spec,
        out_shape=jax.ShapeDtypeStruct((rows_all, HD), jnp.bfloat16),
        compiler_params=pltpu.CompilerParams(
            dimension_semantics=("arbitrary", "arbitrary"),
            vmem_limit_bytes=48 * 1024 * 1024,
        ),
    )(info, q2, *([gathered] * (2 * per_step)), steer2)


def body(queries, keys_values, placement, lengths, steer_index, steering):
    shards = lax.axis_size("ctx")
    my_shard = lax.axis_index("ctx")
    tok_rows = queries.shape[0]
    half_rows = tok_rows // 2
    row_width = queries.shape[1]
    local_heads = row_width // HD
    local_kv = keys_values.shape[2] // HD
    group_size = local_heads // local_kv
    bit_count = shards.bit_length() - 1
    local_rows = jnp.arange(tok_rows, dtype=jnp.int32)
    first_half = local_rows < half_rows
    ends = jnp.cumsum(lengths).astype(jnp.int32)

    mask_rows = jnp.where(first_half, placement[0], placement[1])
    query_pos = jnp.bitwise_xor(my_shard, mask_rows) * tok_rows + local_rows
    qbase = jnp.bitwise_xor(my_shard, placement) * tok_rows + jnp.arange(2, dtype=jnp.int32) * half_rows
    qlast = qbase + half_rows - 1
    qs_first = request_start(qbase, ends)
    qs_last = request_start(qlast, ends)
    info = jnp.concatenate(
        [
            jnp.stack([qbase, qs_first // BK, qlast // BK, qs_last], axis=1).reshape(-1),
            ends,
            placement,
        ]
    ).astype(jnp.int32)

    gathered = lax.all_gather(jnp.transpose(keys_values, (1, 0, 2)), "ctx", axis=0, tiled=False)

    query_request = request_of(query_pos, lengths)
    chosen = steer_index[query_request]
    one_hot = (chosen[:, None] == jnp.arange(steering.shape[0], dtype=jnp.int32)[None, :]).astype(
        jnp.bfloat16
    )
    steer_rows = jnp.dot(one_hot, steering, preferred_element_type=jnp.float32).astype(jnp.bfloat16)

    q2 = queries.reshape(tok_rows * local_heads, HD)
    steer2 = steer_rows.reshape(tok_rows * local_heads, HD)
    out = attention(info, q2, gathered, steer2, group_size).reshape(tok_rows, row_width)

    low_bits = bit_count // 2
    low_count = 1 << low_bits

    def move(piece, m):
        if m == 0:
            return piece
        return lax.ppermute(piece, "ctx", [(d, d ^ m) for d in range(shards)])

    def send(piece, mask):
        low = [functools.partial(move, m=m) for m in range(low_count)]
        high = [functools.partial(move, m=m * low_count) for m in range(shards // low_count)]
        piece = lax.switch(mask % low_count, low, piece)
        return lax.switch(mask // low_count, high, piece)

    halves = [send(out[j * half_rows:(j + 1) * half_rows], placement[j]) for j in range(2)]
    return jnp.concatenate(halves, axis=0)


def solution(mesh):
    return jax.shard_map(
        body,
        mesh=mesh,
        in_specs=(P("ctx", "tp"), P("ctx", None, "tp"), P(), P(), P(), P(None, "tp")),
        out_specs=P("ctx", "tp"),
        check_vma=False,
    )
```

```python
import functools
import math

import jax
import jax.numpy as jnp
from jax import lax
from jax.experimental import pallas as pl
from jax.experimental.pallas import tpu as pltpu
from jax.sharding import PartitionSpec as P

HD = 128
MOST = 10922
BK = 512
negative_fill = -1e30
EXP2_SCALE = math.log2(math.e) / math.sqrt(HD)


def partner(value, axis, bit):
    mask = 2**bit
    pairs = [(source, source ^ mask) for source in range(lax.axis_size(axis))]
    return lax.ppermute(value, axis, pairs)


def request_of(positions, lengths):
    request_ends = jnp.cumsum(lengths)
    return jnp.sum((positions[:, None] >= request_ends[None, :]).astype(jnp.int32), axis=1)


def request_start(positions, ends):
    return jnp.max(jnp.where(ends[None, :] <= positions[:, None], ends[None, :], 0), axis=1)


def attention_kernel(group, steps, info_ref, q_ref, *refs):
    per_step = (len(refs) - 7) // 2
    k_refs, v_refs = refs[:per_step], refs[per_step:2 * per_step]
    steer_ref, o_ref, m_sc, l_sc, acc_sc, qpos_sc, qstart_sc = refs[2 * per_step:]
    j = pl.program_id(0)
    i = pl.program_id(1)
    rows = q_ref.shape[0]
    qbase = info_ref[j * 4 + 0]
    kstart = info_ref[j * 4 + 1]
    kend = info_ref[j * 4 + 2]
    qs_max = info_ref[j * 4 + 3]
    ends = [info_ref[8 + r] for r in range(8)]
    kb = kstart + i

    @pl.when(i == 0)
    def _():
        m_sc[...] = jnp.full(m_sc.shape, negative_fill, jnp.float32)
        l_sc[...] = jnp.zeros(l_sc.shape, jnp.float32)
        acc_sc[...] = jnp.zeros(acc_sc.shape, jnp.float32)
        qpos = qbase + lax.broadcasted_iota(jnp.int32, qpos_sc.shape, 0) // group
        qstart = jnp.zeros(qpos_sc.shape, jnp.int32)
        for e in ends:
            qstart = jnp.where(e <= qpos, jnp.maximum(qstart, e), qstart)
        qpos_sc[...] = qpos
        qstart_sc[...] = qstart

    def step(masked):
        q = q_ref[...]
        k = jnp.concatenate([r[...] for r in k_refs], axis=0)
        v = jnp.concatenate([r[...] for r in v_refs], axis=0)
        s = lax.dot_general(q, k, (((1,), (1,)), ((), ())), preferred_element_type=jnp.float32)
        if masked:
            reps = BK // qpos_sc.shape[1]
            qpos = jnp.tile(qpos_sc[...], (1, reps))
            qstart = jnp.tile(qstart_sc[...], (1, reps))
            kpos = kb * BK + lax.broadcasted_iota(jnp.int32, (1, BK), 1)
            allowed = (kpos <= qpos) & (kpos >= qstart)
            s = jnp.where(allowed, s, negative_fill)
        m_old = m_sc[...]
        reps = s.shape[1] // m_old.shape[1]
        m_new = jnp.maximum(m_old, jnp.max(s, axis=1, keepdims=True))
        p = jnp.exp2((s - jnp.tile(m_new, (1, reps))) * EXP2_SCALE)
        if masked:
            p = jnp.where(allowed, p, 0.0)
        alpha = jnp.exp2((m_old - m_new) * EXP2_SCALE)
        l_sc[...] = alpha * l_sc[...] + jnp.sum(p, axis=1, keepdims=True)
        acc_sc[...] = alpha * acc_sc[...] + jnp.dot(
            p.astype(jnp.bfloat16), v, preferred_element_type=jnp.float32
        )
        m_sc[...] = m_new

    live = kb <= kend
    full = (kb * BK >= qs_max) & ((kb + 1) * BK - 1 <= qbase)

    @pl.when(live & full)
    def _():
        step(False)

    @pl.when(live & jnp.logical_not(full))
    def _():
        step(True)

    @pl.when(i == steps - 1)
    def _():
        attended = (acc_sc[...] / l_sc[...]).astype(jnp.bfloat16).astype(jnp.float32)
        o_ref[...] = (attended + steer_ref[...].astype(jnp.float32)).astype(o_ref.dtype)


def attention(info, q2, gathered, steer2, group):
    rows_all = q2.shape[0]
    half = rows_all // 2
    shards, _, tok_rows, _ = gathered.shape
    sub = tok_rows // 2
    per_step = BK // sub
    total_blocks = shards * tok_rows // BK
    steps = min(total_blocks, (MOST + half // group - 1) // BK + 2)

    def kv_spec(c, kv):
        def index_map(j, i, info_ref):
            kb = jnp.minimum(info_ref[j * 4 + 1] + i, info_ref[j * 4 + 2])
            b = kb * per_step + c
            return (jnp.bitwise_xor(b // 2, info_ref[16 + c % 2]), kv, c % 2, 0)

        return pl.BlockSpec((None, None, sub, HD), index_map)

    grid_spec = pltpu.PrefetchScalarGridSpec(
        num_scalar_prefetch=1,
        grid=(2, steps),
        in_specs=[
            pl.BlockSpec((half, HD), lambda j, i, info_ref: (j, 0)),
            *[kv_spec(c, 0) for c in range(per_step)],
            *[kv_spec(c, 1) for c in range(per_step)],
            pl.BlockSpec((half, HD), lambda j, i, info_ref: (j, 0)),
        ],
        out_specs=pl.BlockSpec((half, HD), lambda j, i, info_ref: (j, 0)),
        scratch_shapes=[
            pltpu.VMEM((half, HD), jnp.float32),
            pltpu.VMEM((half, HD), jnp.float32),
            pltpu.VMEM((half, HD), jnp.float32),
            pltpu.VMEM((half, HD), jnp.int32),
            pltpu.VMEM((half, HD), jnp.int32),
        ],
    )
    return pl.pallas_call(
        functools.partial(attention_kernel, group, steps),
        grid_spec=grid_spec,
        out_shape=jax.ShapeDtypeStruct((rows_all, HD), jnp.bfloat16),
        compiler_params=pltpu.CompilerParams(
            dimension_semantics=("arbitrary", "arbitrary"),
            vmem_limit_bytes=48 * 1024 * 1024,
        ),
    )(info, q2, *([gathered] * (2 * per_step)), steer2)


def body(queries, keys_values, placement, lengths, steer_index, steering):
    shards = lax.axis_size("ctx")
    my_shard = lax.axis_index("ctx")
    tok_rows = queries.shape[0]
    half_rows = tok_rows // 2
    row_width = queries.shape[1]
    local_heads = row_width // HD
    local_kv = keys_values.shape[2] // HD
    group_size = local_heads // local_kv
    bit_count = shards.bit_length() - 1
    local_rows = jnp.arange(tok_rows, dtype=jnp.int32)
    first_half = local_rows < half_rows
    ends = jnp.cumsum(lengths).astype(jnp.int32)

    mask_rows = jnp.where(first_half, placement[0], placement[1])
    query_pos = jnp.bitwise_xor(my_shard, mask_rows) * tok_rows + local_rows
    qbase = jnp.bitwise_xor(my_shard, placement) * tok_rows + jnp.arange(2, dtype=jnp.int32) * half_rows
    qlast = qbase + half_rows - 1
    qs_first = request_start(qbase, ends)
    qs_last = request_start(qlast, ends)
    info = jnp.concatenate(
        [
            jnp.stack([qbase, qs_first // BK, qlast // BK, qs_last], axis=1).reshape(-1),
            ends,
            placement,
        ]
    ).astype(jnp.int32)

    gathered = lax.all_gather(jnp.transpose(keys_values, (1, 0, 2)), "ctx", axis=0, tiled=False)

    query_request = request_of(query_pos, lengths)
    chosen = steer_index[query_request]
    one_hot = (chosen[:, None] == jnp.arange(steering.shape[0], dtype=jnp.int32)[None, :]).astype(
        jnp.bfloat16
    )
    steer_rows = jnp.dot(one_hot, steering, preferred_element_type=jnp.float32).astype(jnp.bfloat16)

    q2 = queries.reshape(tok_rows * local_heads, HD)
    steer2 = steer_rows.reshape(tok_rows * local_heads, HD)
    out = attention(info, q2, gathered, steer2, group_size).reshape(tok_rows, row_width)

    def send(piece, mask):
        branches = [
            functools.partial(
                lambda m, x: lax.ppermute(x, "ctx", [(d, d ^ m) for d in range(shards)]), m
            )
            for m in range(1, shards)
        ]
        return lax.switch(mask - 1, branches, piece)

    halves = [send(out[j * half_rows:(j + 1) * half_rows], placement[j]) for j in range(2)]
    return jnp.concatenate(halves, axis=0)


def solution(mesh):
    return jax.shard_map(
        body,
        mesh=mesh,
        in_specs=(P("ctx", "tp"), P("ctx", None, "tp"), P(), P(), P(), P(None, "tp")),
        out_specs=P("ctx", "tp"),
        check_vma=False,
    )
```

```python
import functools

import jax
import jax.numpy as jnp
from jax import lax
from jax.experimental import pallas as pl
from jax.experimental.pallas import tpu as pltpu
from jax.sharding import PartitionSpec as P

HD = 128
MOST = 10922
BK = 512
negative_fill = -1e30


def partner(value, axis, bit):
    mask = 2**bit
    pairs = [(source, source ^ mask) for source in range(lax.axis_size(axis))]
    return lax.ppermute(value, axis, pairs)


def request_of(positions, lengths):
    request_ends = jnp.cumsum(lengths)
    return jnp.sum((positions[:, None] >= request_ends[None, :]).astype(jnp.int32), axis=1)


def request_start(positions, ends):
    return jnp.max(jnp.where(ends[None, :] <= positions[:, None], ends[None, :], 0), axis=1)


def attention_kernel(group, steps, info_ref, q_ref, *refs):
    per_step = (len(refs) - 7) // 2
    k_refs, v_refs = refs[:per_step], refs[per_step:2 * per_step]
    steer_ref, o_ref, m_sc, l_sc, acc_sc, qpos_sc, qstart_sc = refs[2 * per_step:]
    j = pl.program_id(0)
    i = pl.program_id(1)
    rows = q_ref.shape[0]
    qbase = info_ref[j * 4 + 0]
    kstart = info_ref[j * 4 + 1]
    kend = info_ref[j * 4 + 2]
    qs_max = info_ref[j * 4 + 3]
    ends = [info_ref[8 + r] for r in range(8)]
    kb = kstart + i

    @pl.when(i == 0)
    def _():
        m_sc[...] = jnp.full(m_sc.shape, negative_fill, jnp.float32)
        l_sc[...] = jnp.zeros(l_sc.shape, jnp.float32)
        acc_sc[...] = jnp.zeros(acc_sc.shape, jnp.float32)
        qpos = qbase + lax.broadcasted_iota(jnp.int32, qpos_sc.shape, 0) // group
        qstart = jnp.zeros(qpos_sc.shape, jnp.int32)
        for e in ends:
            qstart = jnp.where(e <= qpos, jnp.maximum(qstart, e), qstart)
        qpos_sc[...] = qpos
        qstart_sc[...] = qstart

    def step(causal, request):
        masked = causal or request
        q = q_ref[...]
        k = jnp.concatenate([r[...] for r in k_refs], axis=0)
        v = jnp.concatenate([r[...] for r in v_refs], axis=0)
        s = lax.dot_general(q, k, (((1,), (1,)), ((), ())), preferred_element_type=jnp.float32)
        if masked:
            reps = BK // qpos_sc.shape[1]
            kpos = kb * BK + lax.broadcasted_iota(jnp.int32, (1, BK), 1)
            allowed = None
            if causal:
                allowed = kpos <= jnp.tile(qpos_sc[...], (1, reps))
            if request:
                after_start = kpos >= jnp.tile(qstart_sc[...], (1, reps))
                allowed = after_start if allowed is None else allowed & after_start
            s = jnp.where(allowed, s, negative_fill)
        m_old = m_sc[...]
        reps = s.shape[1] // m_old.shape[1]
        m_new = jnp.maximum(m_old, jnp.max(s, axis=1, keepdims=True))
        p = jnp.exp((s - jnp.tile(m_new, (1, reps))) * (HD ** -0.5))
        if masked:
            p = jnp.where(allowed, p, 0.0)
        alpha = jnp.exp((m_old - m_new) * (HD ** -0.5))
        l_sc[...] = alpha * l_sc[...] + jnp.sum(p, axis=1, keepdims=True)
        acc_sc[...] = alpha * acc_sc[...] + jnp.dot(
            p.astype(jnp.bfloat16), v, preferred_element_type=jnp.float32
        )
        m_sc[...] = m_new

    live = kb <= kend
    below = (kb + 1) * BK - 1 <= qbase
    inside = kb * BK >= qs_max

    @pl.when(live & below & inside)
    def _():
        step(False, False)

    @pl.when(live & jnp.logical_not(below) & inside)
    def _():
        step(True, False)

    @pl.when(live & below & jnp.logical_not(inside))
    def _():
        step(False, True)

    @pl.when(live & jnp.logical_not(below) & jnp.logical_not(inside))
    def _():
        step(True, True)

    @pl.when(i == steps - 1)
    def _():
        attended = (acc_sc[...] / l_sc[...]).astype(jnp.bfloat16).astype(jnp.float32)
        o_ref[...] = (attended + steer_ref[...].astype(jnp.float32)).astype(o_ref.dtype)


def attention(info, q2, gathered, steer2, group):
    rows_all = q2.shape[0]
    half = rows_all // 2
    shards, _, tok_rows, _ = gathered.shape
    sub = tok_rows // 2
    per_step = BK // sub
    total_blocks = shards * tok_rows // BK
    steps = min(total_blocks, (MOST + half // group - 1) // BK + 2)

    def kv_spec(c, kv):
        def index_map(j, i, info_ref):
            kb = jnp.minimum(info_ref[j * 4 + 1] + i, info_ref[j * 4 + 2])
            b = kb * per_step + c
            return (jnp.bitwise_xor(b // 2, info_ref[16 + c % 2]), kv, c % 2, 0)

        return pl.BlockSpec((None, None, sub, HD), index_map)

    grid_spec = pltpu.PrefetchScalarGridSpec(
        num_scalar_prefetch=1,
        grid=(2, steps),
        in_specs=[
            pl.BlockSpec((half, HD), lambda j, i, info_ref: (j, 0)),
            *[kv_spec(c, 0) for c in range(per_step)],
            *[kv_spec(c, 1) for c in range(per_step)],
            pl.BlockSpec((half, HD), lambda j, i, info_ref: (j, 0)),
        ],
        out_specs=pl.BlockSpec((half, HD), lambda j, i, info_ref: (j, 0)),
        scratch_shapes=[
            pltpu.VMEM((half, HD), jnp.float32),
            pltpu.VMEM((half, HD), jnp.float32),
            pltpu.VMEM((half, HD), jnp.float32),
            pltpu.VMEM((half, HD), jnp.int32),
            pltpu.VMEM((half, HD), jnp.int32),
        ],
    )
    return pl.pallas_call(
        functools.partial(attention_kernel, group, steps),
        grid_spec=grid_spec,
        out_shape=jax.ShapeDtypeStruct((rows_all, HD), jnp.bfloat16),
        compiler_params=pltpu.CompilerParams(
            dimension_semantics=("arbitrary", "arbitrary"),
            vmem_limit_bytes=48 * 1024 * 1024,
        ),
    )(info, q2, *([gathered] * (2 * per_step)), steer2)


def body(queries, keys_values, placement, lengths, steer_index, steering):
    shards = lax.axis_size("ctx")
    my_shard = lax.axis_index("ctx")
    tok_rows = queries.shape[0]
    half_rows = tok_rows // 2
    row_width = queries.shape[1]
    local_heads = row_width // HD
    local_kv = keys_values.shape[2] // HD
    group_size = local_heads // local_kv
    bit_count = shards.bit_length() - 1
    local_rows = jnp.arange(tok_rows, dtype=jnp.int32)
    first_half = local_rows < half_rows
    ends = jnp.cumsum(lengths).astype(jnp.int32)

    mask_rows = jnp.where(first_half, placement[0], placement[1])
    query_pos = jnp.bitwise_xor(my_shard, mask_rows) * tok_rows + local_rows
    qbase = jnp.bitwise_xor(my_shard, placement) * tok_rows + jnp.arange(2, dtype=jnp.int32) * half_rows
    qlast = qbase + half_rows - 1
    qs_first = request_start(qbase, ends)
    qs_last = request_start(qlast, ends)
    info = jnp.concatenate(
        [
            jnp.stack([qbase, qs_first // BK, qlast // BK, qs_last], axis=1).reshape(-1),
            ends,
            placement,
        ]
    ).astype(jnp.int32)

    gathered = lax.all_gather(jnp.transpose(keys_values, (1, 0, 2)), "ctx", axis=0, tiled=False)

    query_request = request_of(query_pos, lengths)
    chosen = steer_index[query_request]
    one_hot = (chosen[:, None] == jnp.arange(steering.shape[0], dtype=jnp.int32)[None, :]).astype(
        jnp.bfloat16
    )
    steer_rows = jnp.dot(one_hot, steering, preferred_element_type=jnp.float32).astype(jnp.bfloat16)

    q2 = queries.reshape(tok_rows * local_heads, HD)
    steer2 = steer_rows.reshape(tok_rows * local_heads, HD)
    out = attention(info, q2, gathered, steer2, group_size).reshape(tok_rows, row_width)

    low_bits = bit_count // 2
    low_count = 1 << low_bits

    def move(piece, m):
        if m == 0:
            return piece
        return lax.ppermute(piece, "ctx", [(d, d ^ m) for d in range(shards)])

    def send(piece, mask):
        low = [functools.partial(move, m=m) for m in range(low_count)]
        high = [functools.partial(move, m=m * low_count) for m in range(shards // low_count)]
        piece = lax.switch(mask % low_count, low, piece)
        return lax.switch(mask // low_count, high, piece)

    halves = [send(out[j * half_rows:(j + 1) * half_rows], placement[j]) for j in range(2)]
    return jnp.concatenate(halves, axis=0)


def solution(mesh):
    return jax.shard_map(
        body,
        mesh=mesh,
        in_specs=(P("ctx", "tp"), P("ctx", None, "tp"), P(), P(), P(), P(None, "tp")),
        out_specs=P("ctx", "tp"),
        check_vma=False,
    )
```

```python
import functools
import math

import jax
import jax.numpy as jnp
from jax import lax
from jax.experimental import pallas as pl
from jax.experimental.pallas import tpu as pltpu
from jax.sharding import PartitionSpec as P

HD = 128
MOST = 10922
BK = 512
negative_fill = -1e30
EXP2_SCALE = math.log2(math.e) / math.sqrt(HD)


def partner(value, axis, bit):
    mask = 2**bit
    pairs = [(source, source ^ mask) for source in range(lax.axis_size(axis))]
    return lax.ppermute(value, axis, pairs)


def request_of(positions, lengths):
    request_ends = jnp.cumsum(lengths)
    return jnp.sum((positions[:, None] >= request_ends[None, :]).astype(jnp.int32), axis=1)


def request_start(positions, ends):
    return jnp.max(jnp.where(ends[None, :] <= positions[:, None], ends[None, :], 0), axis=1)


def attention_kernel(group, steps, info_ref, q_ref, *refs):
    per_step = (len(refs) - 7) // 2
    k_refs, v_refs = refs[:per_step], refs[per_step:2 * per_step]
    steer_ref, o_ref, m_sc, l_sc, acc_sc, qpos_sc, qstart_sc = refs[2 * per_step:]
    j = pl.program_id(0)
    i = pl.program_id(1)
    rows = q_ref.shape[0]
    qbase = info_ref[j * 4 + 0]
    kstart = info_ref[j * 4 + 1]
    kend = info_ref[j * 4 + 2]
    qs_max = info_ref[j * 4 + 3]
    ends = [info_ref[8 + r] for r in range(8)]
    kb = kstart + i

    @pl.when(i == 0)
    def _():
        m_sc[...] = jnp.full(m_sc.shape, negative_fill, jnp.float32)
        l_sc[...] = jnp.zeros(l_sc.shape, jnp.float32)
        acc_sc[...] = jnp.zeros(acc_sc.shape, jnp.float32)
        qpos = qbase + lax.broadcasted_iota(jnp.int32, qpos_sc.shape, 0) // group
        qstart = jnp.zeros(qpos_sc.shape, jnp.int32)
        for e in ends:
            qstart = jnp.where(e <= qpos, jnp.maximum(qstart, e), qstart)
        qpos_sc[...] = qpos
        qstart_sc[...] = qstart

    def step(causal, request):
        masked = causal or request
        q = q_ref[...]
        k = jnp.concatenate([r[...] for r in k_refs], axis=0)
        v = jnp.concatenate([r[...] for r in v_refs], axis=0)
        s = lax.dot_general(q, k, (((1,), (1,)), ((), ())), preferred_element_type=jnp.float32)
        if masked:
            reps = BK // qpos_sc.shape[1]
            kpos = kb * BK + lax.broadcasted_iota(jnp.int32, (1, BK), 1)
            allowed = None
            if causal:
                allowed = kpos <= jnp.tile(qpos_sc[...], (1, reps))
            if request:
                after_start = kpos >= jnp.tile(qstart_sc[...], (1, reps))
                allowed = after_start if allowed is None else allowed & after_start
            s = jnp.where(allowed, s, negative_fill)
        m_old = m_sc[...]
        reps = s.shape[1] // m_old.shape[1]
        m_new = jnp.maximum(m_old, jnp.max(s, axis=1, keepdims=True))
        p = jnp.exp2((s - jnp.tile(m_new, (1, reps))) * EXP2_SCALE)
        if masked:
            p = jnp.where(allowed, p, 0.0)
        alpha = jnp.exp2((m_old - m_new) * EXP2_SCALE)
        l_sc[...] = alpha * l_sc[...] + jnp.sum(p, axis=1, keepdims=True)
        acc_sc[...] = alpha * acc_sc[...] + jnp.dot(
            p.astype(jnp.bfloat16), v, preferred_element_type=jnp.float32
        )
        m_sc[...] = m_new

    live = kb <= kend
    below = (kb + 1) * BK - 1 <= qbase
    inside = kb * BK >= qs_max

    @pl.when(live & below & inside)
    def _():
        step(False, False)

    @pl.when(live & jnp.logical_not(below) & inside)
    def _():
        step(True, False)

    @pl.when(live & below & jnp.logical_not(inside))
    def _():
        step(False, True)

    @pl.when(live & jnp.logical_not(below) & jnp.logical_not(inside))
    def _():
        step(True, True)

    @pl.when(i == steps - 1)
    def _():
        attended = (acc_sc[...] / l_sc[...]).astype(jnp.bfloat16).astype(jnp.float32)
        o_ref[...] = (attended + steer_ref[...].astype(jnp.float32)).astype(o_ref.dtype)


def attention(info, q2, gathered, steer2, group):
    rows_all = q2.shape[0]
    half = rows_all // 2
    shards, _, tok_rows, _ = gathered.shape
    sub = tok_rows // 2
    per_step = BK // sub
    total_blocks = shards * tok_rows // BK
    steps = min(total_blocks, (MOST + half // group - 1) // BK + 2)

    def kv_spec(c, kv):
        def index_map(j, i, info_ref):
            kb = jnp.minimum(info_ref[j * 4 + 1] + i, info_ref[j * 4 + 2])
            b = kb * per_step + c
            return (jnp.bitwise_xor(b // 2, info_ref[16 + c % 2]), kv, c % 2, 0)

        return pl.BlockSpec((None, None, sub, HD), index_map)

    grid_spec = pltpu.PrefetchScalarGridSpec(
        num_scalar_prefetch=1,
        grid=(2, steps),
        in_specs=[
            pl.BlockSpec((half, HD), lambda j, i, info_ref: (j, 0)),
            *[kv_spec(c, 0) for c in range(per_step)],
            *[kv_spec(c, 1) for c in range(per_step)],
            pl.BlockSpec((half, HD), lambda j, i, info_ref: (j, 0)),
        ],
        out_specs=pl.BlockSpec((half, HD), lambda j, i, info_ref: (j, 0)),
        scratch_shapes=[
            pltpu.VMEM((half, HD), jnp.float32),
            pltpu.VMEM((half, HD), jnp.float32),
            pltpu.VMEM((half, HD), jnp.float32),
            pltpu.VMEM((half, HD), jnp.int32),
            pltpu.VMEM((half, HD), jnp.int32),
        ],
    )
    return pl.pallas_call(
        functools.partial(attention_kernel, group, steps),
        grid_spec=grid_spec,
        out_shape=jax.ShapeDtypeStruct((rows_all, HD), jnp.bfloat16),
        compiler_params=pltpu.CompilerParams(
            dimension_semantics=("arbitrary", "arbitrary"),
            vmem_limit_bytes=48 * 1024 * 1024,
        ),
    )(info, q2, *([gathered] * (2 * per_step)), steer2)


def body(queries, keys_values, placement, lengths, steer_index, steering):
    shards = lax.axis_size("ctx")
    my_shard = lax.axis_index("ctx")
    tok_rows = queries.shape[0]
    half_rows = tok_rows // 2
    row_width = queries.shape[1]
    local_heads = row_width // HD
    local_kv = keys_values.shape[2] // HD
    group_size = local_heads // local_kv
    bit_count = shards.bit_length() - 1
    local_rows = jnp.arange(tok_rows, dtype=jnp.int32)
    first_half = local_rows < half_rows
    ends = jnp.cumsum(lengths).astype(jnp.int32)

    mask_rows = jnp.where(first_half, placement[0], placement[1])
    query_pos = jnp.bitwise_xor(my_shard, mask_rows) * tok_rows + local_rows
    qbase = jnp.bitwise_xor(my_shard, placement) * tok_rows + jnp.arange(2, dtype=jnp.int32) * half_rows
    qlast = qbase + half_rows - 1
    qs_first = request_start(qbase, ends)
    qs_last = request_start(qlast, ends)
    info = jnp.concatenate(
        [
            jnp.stack([qbase, qs_first // BK, qlast // BK, qs_last], axis=1).reshape(-1),
            ends,
            placement,
        ]
    ).astype(jnp.int32)

    gathered = lax.all_gather(jnp.transpose(keys_values, (1, 0, 2)), "ctx", axis=0, tiled=False)

    query_request = request_of(query_pos, lengths)
    chosen = steer_index[query_request]
    one_hot = (chosen[:, None] == jnp.arange(steering.shape[0], dtype=jnp.int32)[None, :]).astype(
        jnp.bfloat16
    )
    steer_rows = jnp.dot(one_hot, steering, preferred_element_type=jnp.float32).astype(jnp.bfloat16)

    q2 = queries.reshape(tok_rows * local_heads, HD)
    steer2 = steer_rows.reshape(tok_rows * local_heads, HD)
    out = attention(info, q2, gathered, steer2, group_size).reshape(tok_rows, row_width)

    low_bits = bit_count // 2
    low_count = 1 << low_bits

    def move(piece, m):
        if m == 0:
            return piece
        return lax.ppermute(piece, "ctx", [(d, d ^ m) for d in range(shards)])

    def send(piece, mask):
        low = [functools.partial(move, m=m) for m in range(low_count)]
        high = [functools.partial(move, m=m * low_count) for m in range(shards // low_count)]
        piece = lax.switch(mask % low_count, low, piece)
        return lax.switch(mask // low_count, high, piece)

    halves = [send(out[j * half_rows:(j + 1) * half_rows], placement[j]) for j in range(2)]
    return jnp.concatenate(halves, axis=0)


def solution(mesh):
    return jax.shard_map(
        body,
        mesh=mesh,
        in_specs=(P("ctx", "tp"), P("ctx", None, "tp"), P(), P(), P(), P(None, "tp")),
        out_specs=P("ctx", "tp"),
        check_vma=False,
    )
```
